128 devices in a mesh: group: 4 (over z), dev: 32 (over y, x, core).
Axes of the slice: x: 4, y: 4, z: 4, core: 2. Of those that a mesh axis runs over, the one named last changes fastest.
Arguments:
- tokens: bfloat16 [16384, 3584], P(('group', 'dev')), may hold values from -1.5 to 1.5
- out_grad: bfloat16 [16384, 3584], P(('group', 'dev')), may hold values from -0.59765625 to 0.59765625
- gate_weights: bfloat16 [16384, 8], P(('group', 'dev')), may hold values from 0.099609375 to 1
- expert_ids: int32 [16384, 8], P(('group', 'dev')), may hold values from 0 to 127, as said below
- slot_ids: int32 [16384, 8], P(('group', 'dev')), may hold values from 0 to 9, as said below
- up_weight: bfloat16 [128, 3584, 1024], P(('group', 'dev')), may hold values from -0.40039062 to 0.40039062
- down_weight: bfloat16 [128, 1024, 3584], P(('group', 'dev')), may hold values from -0.1875 to 0.1875
Outputs:
- token_grad: bfloat16 [16384, 3584], P(('group', 'dev'))
- gate_grad: bfloat16 [16384, 8], P(('group', 'dev'))
The draws below stay inside these ranges and needn't reach their ends.
Inputs may be any that keep to these rules, and one draw needn't show every extreme that they name: `expert_ids`: expert e lies in group e // 32 and on the device of index e along group+dev. Each token names 8 different experts, 4 in each of exactly 2 groups. In the rows of one device no expert is named more than 10 times and some expert exactly 10 times; no group is named by more than 80 rows and some group by exactly 80. `slot_ids`: in the rows of one device, two entries that name the same expert have different slots.
All inputs are finite; a program needn't handle non-finite values.
Results may differ from the reference program's by a relative error of at most 0.009.
Values may be sent and summed in bfloat16 or wider, within the bound.
No kernel may reach another device: no remote copies, remote signals or barrier semaphores. Data moves between devices by JAX's collectives and lax.ppermute only.
A program may use at most 192 MiB of HBM per device.

```python
import math
import jax
import jax.numpy as jnp
from jax import lax

D = 3584
H = 1024
TOPK = 8
TOK_DEV = 128
GROUPS = 4
EXP_GROUP = 32
EXPERTS = 128
TOKENS = 16384
EPG = 4
MOST = 10
GROUP_ROWS = 80
DEVICES = 128


def route_tables(key):
    key = jax.random.fold_in(key, 11)
    key_list = jax.random.split(key, 4)
    blocks = TOKENS // TOK_DEV
    home_group = jax.random.randint(key_list[0], (blocks, 1), 0, GROUPS)
    token_order = jnp.argsort(jax.random.randint(key_list[1], (blocks, TOK_DEV), 0, 1 << 20) * TOK_DEV + jnp.arange(TOK_DEV), axis=1)
    token_rank = jnp.argsort(token_order, axis=1)
    rank_pos = jnp.arange(TOK_DEV)[None, :]
    other_count = GROUPS - 1
    with_home = rank_pos < GROUP_ROWS
    rotation = (rank_pos - GROUP_ROWS) % other_count
    group_one = jnp.where(with_home, home_group, (home_group + 1 + rotation) % GROUPS)
    group_two = jnp.where(with_home, (home_group + 1 + rank_pos % other_count) % GROUPS, (home_group + 1 + (rotation + 1) % other_count) % GROUPS)
    group_ids = jnp.arange(GROUPS)
    names_group = ((group_one[:, :, None] == group_ids) | (group_two[:, :, None] == group_ids)).astype(jnp.int32)
    group_rank = jnp.cumsum(names_group, axis=1) - 1
    expert_order = jnp.argsort(jax.random.randint(key_list[2], (blocks, GROUPS, EXP_GROUP), 0, 1 << 20) * EXP_GROUP + jnp.arange(EXP_GROUP), axis=2)
    pick_off = jnp.arange(EPG)[None, None, :]
    block_ids = jnp.arange(blocks)[:, None]

    def picks(chosen):
        order_pos = jnp.take_along_axis(group_rank, chosen[:, :, None], axis=2)
        pick_pos = order_pos * EPG + pick_off
        members = expert_order[block_ids, chosen]
        local_ids = jnp.take_along_axis(members, pick_pos % EXP_GROUP, axis=2)
        return (chosen[:, :, None] * EXP_GROUP + local_ids, pick_pos // EXP_GROUP)
    ids_one, slot_one = picks(group_one)
    ids_two, slot_two = picks(group_two)
    ids_rank = jnp.concatenate([ids_one, ids_two], axis=2)
    slot_rank = jnp.concatenate([slot_one, slot_two], axis=2)
    entry_order = jnp.argsort(jax.random.randint(key_list[3], (blocks, TOK_DEV, TOPK), 0, 1 << 20) * TOPK + jnp.arange(TOPK), axis=2)
    ids_rank = jnp.take_along_axis(ids_rank, entry_order, axis=2)
    slot_rank = jnp.take_along_axis(slot_rank, entry_order, axis=2)
    ids_token = jnp.take_along_axis(ids_rank, token_rank[:, :, None], axis=1)
    slot_token = jnp.take_along_axis(slot_rank, token_rank[:, :, None], axis=1)
    return (ids_token.reshape(TOKENS, TOPK).astype(jnp.int32), slot_token.reshape(TOKENS, TOPK).astype(jnp.int32))


def draw_expert_ids(key, part):
    return route_tables(key)[0]


def draw_slot_ids(key, part):
    return route_tables(key)[1]


def steps_of(own_key, extent, pieces, least, largest):
    def one(dim, shards_of):
        heights = jax.random.uniform(jax.random.fold_in(jax.random.fold_in(own_key, 6), dim), (shards_of,), jnp.float32, least / len(pieces), largest / len(pieces))
        return jnp.repeat(jnp.exp(heights), extent[dim] // shards_of).reshape((-1,) + (1,) * (len(extent) - dim - 1))

    level = one(*pieces[0])
    for cut in pieces[1:]:
        level = level * one(*cut)
    return level


def bell_draw(own_key, extent, deviation, limit, cuts=(), held_as=jnp.bfloat16):
    values = deviation * jax.random.normal(own_key, extent, jnp.float32)
    if cuts:
        values = values * steps_of(own_key, extent, cuts, -0.22, 0.18)
    return jnp.clip(values, -limit, limit).astype(held_as)


def setup_inputs(seed: int = 0) -> dict:
    keys = jax.random.split(jax.random.key(seed), 8)
    tokens = bell_draw(keys[0], (TOKENS, D), 0.25, 1.5, ((0, 128),))
    out_grad = bell_draw(keys[1], (TOKENS, D), 0.1, 0.59765625, ((0, 128),))
    gate_weights = jnp.clip(jnp.exp(math.log(1.0) - 2.306499 * jax.random.uniform(keys[2], (TOKENS, TOPK), jnp.float32) ** steps_of(keys[2], (TOKENS, TOPK), ((0, 128),), -0.2, 0.2)), 0.099609375, 1.0).astype(jnp.bfloat16)
    expert_ids = draw_expert_ids(jax.random.fold_in(keys[7], 71), 0)
    slot_ids = draw_slot_ids(jax.random.fold_in(keys[7], 71), 0)
    up_weight = bell_draw(keys[5], (EXPERTS, D, H), (4.0 / D ** 0.5), 0.40039062, ((0, 128),))
    down_weight = bell_draw(keys[6], (EXPERTS, H, D), H ** -0.5, 0.1875, ((0, 128),))
    return dict(tokens=tokens, out_grad=out_grad, gate_weights=gate_weights, expert_ids=expert_ids, slot_ids=slot_ids, up_weight=up_weight, down_weight=down_weight)


def silu_slope(values):
    sigmoid_up = jax.nn.sigmoid(values)
    return sigmoid_up * (1.0 + values * (1.0 - sigmoid_up))


def expert_rows(token_rows, grad_rows, gate_rows, up_matrix, down_matrix):
    raised = jnp.dot(token_rows, up_matrix, preferred_element_type=jnp.float32)
    backward = lax.dot_general(grad_rows, down_matrix, (((1,), (1,)), ((), ())), preferred_element_type=jnp.float32)
    gate_grad = jnp.sum(jax.nn.silu(raised) * backward, axis=1).astype(jnp.bfloat16)
    inner_grad = (gate_rows.astype(jnp.float32)[:, None] * backward * silu_slope(raised)).astype(jnp.bfloat16)
    contrib = lax.dot_general(inner_grad, up_matrix, (((1,), (1,)), ((), ())), preferred_element_type=jnp.float32).astype(jnp.bfloat16)
    return contrib, gate_grad


def reference(tokens, out_grad, gate_weights, expert_ids, slot_ids, up_weight, down_weight):
    entries = TOKENS * TOPK
    source = (jnp.arange(TOKENS, dtype=jnp.int32) // TOK_DEV)[:, None]
    flat_slot = ((expert_ids * DEVICES + source) * MOST + slot_ids).reshape(-1).astype(jnp.int32)
    slot_table = jnp.full((EXPERTS * DEVICES * MOST,), entries, jnp.int32)
    slot_table = slot_table.at[flat_slot].set(jnp.arange(entries, dtype=jnp.int32))
    slot_table = slot_table.reshape(EXPERTS, DEVICES * MOST)
    group_of = expert_ids // EXP_GROUP
    other_half = jnp.where(group_of == group_of[:, :1], 0, 1).astype(jnp.int32).reshape(-1)
    half_pad = jnp.concatenate([other_half, jnp.zeros((1,), jnp.int32)])
    token_pad = jnp.concatenate([tokens, jnp.zeros((1, D), jnp.bfloat16)])
    grad_pad = jnp.concatenate([out_grad, jnp.zeros((1, D), jnp.bfloat16)])
    gate_pad = jnp.concatenate([gate_weights.reshape(-1), jnp.zeros((1,), jnp.bfloat16)])

    def expert_step(carried, inputs):
        summed, gate_out = carried
        entry_row, up_matrix, down_matrix = inputs
        anchor = (entry_row // TOPK).astype(jnp.int32)
        contrib, gate_rows = expert_rows(token_pad[anchor], grad_pad[anchor], gate_pad[entry_row], up_matrix, down_matrix)
        target = jnp.where(entry_row < entries, half_pad[entry_row] * TOKENS + anchor, 2 * TOKENS).astype(jnp.int32)
        summed = summed.at[target].add(contrib.astype(jnp.float32))
        gate_out = gate_out.at[entry_row].set(gate_rows)
        return (summed, gate_out), None

    start = (jnp.zeros((2 * TOKENS + 1, D), jnp.float32), jnp.zeros((entries + 1,), jnp.bfloat16))
    (summed, gate_out), unused = lax.scan(expert_step, start, (slot_table, up_weight, down_weight))
    halves = lax.optimization_barrier(summed[:2 * TOKENS].astype(jnp.bfloat16))
    halves = halves.astype(jnp.float32).reshape(2, TOKENS, D)
    token_grad = (halves[0] + halves[1]).astype(jnp.bfloat16)
    return token_grad, gate_out[:entries].reshape(TOKENS, TOPK)
```

```python
import jax
import jax.numpy as jnp
from jax import lax
from jax.sharding import PartitionSpec as P

TOPK = 8
LANES = 128


def silu_slope(values):
    sigmoid_up = jax.nn.sigmoid(values)
    return sigmoid_up * (1.0 + values * (1.0 - sigmoid_up))


def expert_rows(token_rows, grad_rows, gate_rows, up_matrix, down_matrix):
    raised = jnp.dot(token_rows, up_matrix, preferred_element_type=jnp.float32)
    backward = lax.dot_general(
        grad_rows, down_matrix, (((1,), (1,)), ((), ())), preferred_element_type=jnp.float32
    )
    gate_grad = jnp.sum(jax.nn.silu(raised) * backward, axis=1).astype(jnp.bfloat16)
    inner_grad = (gate_rows.astype(jnp.float32)[:, None] * backward * silu_slope(raised)).astype(
        jnp.bfloat16
    )
    contrib = lax.dot_general(
        inner_grad, up_matrix, (((1,), (1,)), ((), ())), preferred_element_type=jnp.float32
    ).astype(jnp.bfloat16)
    return (contrib, gate_grad)


def exchange(x):
    return lax.all_to_all(x, ("group", "dev"), split_axis=0, concat_axis=0, tiled=True)


def shards(tokens, out_grad, gate_weights, expert_ids, slot_ids, up_weight, down_weight):
    rows_dev = tokens.shape[0]
    features = tokens.shape[1]
    groups = lax.axis_size("group")
    per_group = lax.axis_size("dev")
    experts = groups * per_group
    capacity = 5 * rows_dev * TOPK // (4 * experts)
    slots_all = experts * capacity
    entries = rows_dev * TOPK
    up_matrix = up_weight[0]
    down_matrix = down_weight[0]
    group_of = expert_ids // per_group
    both = 2 * features
    blocks = both // LANES
    joined = jnp.concatenate(
        [jnp.concatenate([tokens, out_grad], axis=1), jnp.zeros((1, both), jnp.bfloat16)]
    ).reshape(rows_dev + 1, blocks, LANES)
    gate_flat = jnp.concatenate([gate_weights.reshape(-1), jnp.zeros((1,), jnp.bfloat16)])
    target = (expert_ids * capacity + slot_ids).reshape(-1)
    slot_table = (
        jnp.full((slots_all,), entries, jnp.int32)
        .at[target]
        .set(jnp.arange(entries, dtype=jnp.int32))
    )
    anchor = slot_table // TOPK
    sent = joined[anchor].reshape(experts, capacity * blocks, LANES)
    arrived = exchange(sent).reshape(slots_all, both)
    gate_in = exchange(gate_flat[slot_table].reshape(experts, capacity))
    contrib, gate_rows = expert_rows(
        arrived[:, :features],
        arrived[:, features:],
        gate_in.reshape(slots_all),
        up_matrix,
        down_matrix,
    )
    half_blocks = capacity // 2 * both // LANES
    returned = exchange(contrib.reshape(experts, half_blocks, LANES)).reshape(slots_all, features)
    gate_back = exchange(gate_rows.reshape(experts, capacity))
    gathered = returned[target].reshape(rows_dev, TOPK, features)
    gate_grad = gate_back.reshape(-1)[target].reshape(rows_dev, TOPK)
    same_group = group_of == group_of[:, :1]
    selector = jnp.stack([same_group, jnp.logical_not(same_group)], axis=1).astype(jnp.bfloat16)
    halves = jnp.einsum(
        "tpk,tkd->tpd", selector, gathered, preferred_element_type=jnp.float32
    ).astype(jnp.bfloat16)
    token_grad = jnp.sum(halves.astype(jnp.float32), axis=1).astype(jnp.bfloat16)
    return (token_grad, gate_grad)


def solution(mesh):
    in_specs = (
        P(("group", "dev"), None),
        P(("group", "dev"), None),
        P(("group", "dev"), None),
        P(("group", "dev"), None),
        P(("group", "dev"), None),
        P(("group", "dev"), None, None),
        P(("group", "dev"), None, None),
    )
    out_specs = (P(("group", "dev"), None), P(("group", "dev"), None))
    return jax.shard_map(shards, mesh=mesh, in_specs=in_specs, out_specs=out_specs, check_vma=False)
```

```python
import jax
import jax.numpy as jnp
from jax import lax
from jax.sharding import PartitionSpec as P

TOPK = 8
LANES = 128
CHUNKS = 2
BACK_ROWS = 4


def silu_slope(values):
    sigmoid_up = jax.nn.sigmoid(values)
    return sigmoid_up * (1.0 + values * (1.0 - sigmoid_up))


def expert_rows(token_rows, grad_rows, gate_rows, up_matrix, down_matrix):
    raised = jnp.dot(token_rows, up_matrix, preferred_element_type=jnp.float32)
    backward = lax.dot_general(
        grad_rows, down_matrix, (((1,), (1,)), ((), ())), preferred_element_type=jnp.float32
    )
    gate_grad = jnp.sum(jax.nn.silu(raised) * backward, axis=1).astype(jnp.bfloat16)
    inner_grad = (gate_rows.astype(jnp.float32)[:, None] * backward * silu_slope(raised)).astype(
        jnp.bfloat16
    )
    contrib = lax.dot_general(
        inner_grad, up_matrix, (((1,), (1,)), ((), ())), preferred_element_type=jnp.float32
    ).astype(jnp.bfloat16)
    return (contrib, gate_grad)


def exchange(x):
    return lax.all_to_all(x, ("group", "dev"), split_axis=0, concat_axis=0, tiled=True)


def side_block(values, rows):
    n = values.shape[1]
    return jnp.pad(values[:, None, :], ((0, 0), (0, rows - 1), (0, LANES - n)))


def layer(tokens, out_grad, gate_weights, expert_ids, slot_ids, up_weight, down_weight):
    rows_dev = tokens.shape[0]
    features = tokens.shape[1]
    groups = lax.axis_size("group")
    per_group = lax.axis_size("dev")
    experts = groups * per_group
    capacity = 5 * rows_dev * TOPK // (4 * experts)
    slots_all = experts * capacity
    entries = rows_dev * TOPK
    up_matrix = up_weight[0]
    down_matrix = down_weight[0]
    group_of = expert_ids // per_group
    both = 2 * features
    blocks = both // LANES
    part = capacity // CHUNKS
    part_rows = experts * part
    joined = jnp.concatenate(
        [jnp.concatenate([tokens, out_grad], axis=1), jnp.zeros((1, both), jnp.bfloat16)]
    ).reshape(rows_dev + 1, blocks, LANES)
    gate_flat = jnp.concatenate([gate_weights.reshape(-1), jnp.zeros((1,), jnp.bfloat16)])
    target = (expert_ids * capacity + slot_ids).reshape(-1)
    slot_table = (
        jnp.full((slots_all,), entries, jnp.int32)
        .at[target]
        .set(jnp.arange(entries, dtype=jnp.int32))
    ).reshape(experts, capacity)
    gate_all = exchange(gate_flat[slot_table])
    contribs = []
    gate_backs = []
    for c in range(CHUNKS):
        table = slot_table[:, c * part:(c + 1) * part]
        sent = joined[table // TOPK].reshape(experts, part * blocks, LANES)
        arrived = exchange(sent)
        data = arrived.reshape(part_rows, both)
        gate_in = gate_all[:, c * part:(c + 1) * part].reshape(part_rows)
        contrib, gate_rows = expert_rows(
            data[:, :features], data[:, features:], gate_in, up_matrix, down_matrix
        )
        back_blocks = part * features // LANES
        back = jnp.concatenate(
            [
                contrib.reshape(experts, back_blocks, LANES),
                side_block(gate_rows.reshape(experts, part), BACK_ROWS),
            ],
            axis=1,
        )
        returned = exchange(back)
        contribs.append(returned[:, :back_blocks, :].reshape(part_rows, features))
        gate_backs.append(returned[:, back_blocks, :part])
    all_contrib = jnp.concatenate(contribs, axis=0)
    all_gate = jnp.concatenate(gate_backs, axis=1)
    slot_flat = slot_ids.reshape(-1)
    expert_flat = expert_ids.reshape(-1)
    where = (slot_flat // part) * part_rows + expert_flat * part + slot_flat % part
    gathered = all_contrib[where].reshape(rows_dev, TOPK, features)
    gate_grad = all_gate.reshape(-1)[target].reshape(rows_dev, TOPK)
    same_group = group_of == group_of[:, :1]
    selector = jnp.stack([same_group, jnp.logical_not(same_group)], axis=1).astype(jnp.bfloat16)
    halves = jnp.einsum(
        "tpk,tkd->tpd", selector, gathered, preferred_element_type=jnp.float32
    ).astype(jnp.bfloat16)
    token_grad = jnp.sum(halves.astype(jnp.float32), axis=1).astype(jnp.bfloat16)
    return (token_grad, gate_grad)


def solution(mesh):
    in_specs = (
        P(("group", "dev"), None),
        P(("group", "dev"), None),
        P(("group", "dev"), None),
        P(("group", "dev"), None),
        P(("group", "dev"), None),
        P(("group", "dev"), None, None),
        P(("group", "dev"), None, None),
    )
    out_specs = (P(("group", "dev"), None), P(("group", "dev"), None))
    return jax.shard_map(layer, mesh=mesh, in_specs=in_specs, out_specs=out_specs, check_vma=False)
```

```python
import jax
import jax.numpy as jnp
from jax import lax
from jax.sharding import PartitionSpec as P

TOPK = 8
LANES = 128
CHUNKS = 2
BACK_ROWS = 4


def silu_slope(values):
    sigmoid_up = jax.nn.sigmoid(values)
    return sigmoid_up * (1.0 + values * (1.0 - sigmoid_up))


def expert_rows(token_rows, grad_rows, up_matrix, down_matrix):
    raised = jnp.dot(token_rows, up_matrix, preferred_element_type=jnp.float32)
    backward = lax.dot_general(
        grad_rows, down_matrix, (((1,), (1,)), ((), ())), preferred_element_type=jnp.float32
    )
    gate_grad = jnp.sum(jax.nn.silu(raised) * backward, axis=1).astype(jnp.bfloat16)
    inner_grad = (backward * silu_slope(raised)).astype(jnp.bfloat16)
    contrib = lax.dot_general(
        inner_grad, up_matrix, (((1,), (1,)), ((), ())), preferred_element_type=jnp.float32
    ).astype(jnp.bfloat16)
    return (contrib, gate_grad)


def exchange(x):
    return lax.all_to_all(x, ("group", "dev"), split_axis=0, concat_axis=0, tiled=True)


def side_block(values, rows):
    n = values.shape[1]
    return jnp.pad(values[:, None, :], ((0, 0), (0, rows - 1), (0, LANES - n)))


def layer(tokens, out_grad, gate_weights, expert_ids, slot_ids, up_weight, down_weight):
    rows_dev = tokens.shape[0]
    features = tokens.shape[1]
    groups = lax.axis_size("group")
    per_group = lax.axis_size("dev")
    experts = groups * per_group
    capacity = 5 * rows_dev * TOPK // (4 * experts)
    slots_all = experts * capacity
    entries = rows_dev * TOPK
    up_matrix = up_weight[0]
    down_matrix = down_weight[0]
    group_of = expert_ids // per_group
    both = 2 * features
    blocks = both // LANES
    part = capacity // CHUNKS
    part_rows = experts * part
    joined = jnp.concatenate(
        [jnp.concatenate([tokens, out_grad], axis=1), jnp.zeros((1, both), jnp.bfloat16)]
    ).reshape(rows_dev + 1, blocks, LANES)
    target = (expert_ids * capacity + slot_ids).reshape(-1)
    slot_table = (
        jnp.full((slots_all,), entries, jnp.int32)
        .at[target]
        .set(jnp.arange(entries, dtype=jnp.int32))
    ).reshape(experts, capacity)
    slot_flat = slot_ids.reshape(-1)
    expert_flat = expert_ids.reshape(-1)
    same_group = group_of == group_of[:, :1]
    selector = jnp.stack([same_group, jnp.logical_not(same_group)], axis=1)
    gate_rowwise = gate_weights.reshape(rows_dev, 1, TOPK)
    summed = None
    gate_backs = []
    for c in range(CHUNKS):
        table = slot_table[:, c * part:(c + 1) * part]
        sent = joined[table // TOPK].reshape(experts, part * blocks, LANES)
        arrived = exchange(sent)
        data = arrived.reshape(part_rows, both)
        contrib, gate_rows = expert_rows(
            data[:, :features], data[:, features:], up_matrix, down_matrix
        )
        back_blocks = part * features // LANES
        back = jnp.concatenate(
            [
                contrib.reshape(experts, back_blocks, LANES),
                side_block(gate_rows.reshape(experts, part), BACK_ROWS),
            ],
            axis=1,
        )
        returned = exchange(back)
        rows_back = returned[:, :back_blocks, :].reshape(part_rows, features)
        gate_backs.append(returned[:, back_blocks, :part])
        in_chunk = (slot_flat // part == c).reshape(rows_dev, 1, TOPK)
        where = jnp.clip(expert_flat * part + slot_flat - c * part, 0, part_rows - 1)
        gathered = rows_back[where].reshape(rows_dev, TOPK, features)
        pick = jnp.where(jnp.logical_and(selector, in_chunk), gate_rowwise, jnp.bfloat16(0))
        partial = jnp.einsum(
            "tpk,tkd->tpd", pick, gathered, preferred_element_type=jnp.float32
        )
        summed = partial if summed is None else summed + partial
    all_gate = jnp.concatenate(gate_backs, axis=1)
    gate_grad = all_gate.reshape(-1)[target].reshape(rows_dev, TOPK)
    halves = summed.astype(jnp.bfloat16)
    token_grad = jnp.sum(halves.astype(jnp.float32), axis=1).astype(jnp.bfloat16)
    return (token_grad, gate_grad)


def solution(mesh):
    in_specs = (
        P(("group", "dev"), None),
        P(("group", "dev"), None),
        P(("group", "dev"), None),
        P(("group", "dev"), None),
        P(("group", "dev"), None),
        P(("group", "dev"), None, None),
        P(("group", "dev"), None, None),
    )
    out_specs = (P(("group", "dev"), None), P(("group", "dev"), None))
    return jax.shard_map(layer, mesh=mesh, in_specs=in_specs, out_specs=out_specs, check_vma=False)
```

```python
import jax
import jax.numpy as jnp
from jax import lax
from jax.sharding import PartitionSpec as P

TOPK = 8
LANES = 128
CHUNKS = 2
BACK_ROWS = 4


def silu_slope(values):
    sigmoid_up = jax.nn.sigmoid(values)
    return sigmoid_up * (1.0 + values * (1.0 - sigmoid_up))


def expert_rows(token_rows, grad_rows, up_matrix, down_matrix):
    raised = jnp.dot(token_rows, up_matrix, preferred_element_type=jnp.float32)
    backward = lax.dot_general(
        grad_rows, down_matrix, (((1,), (1,)), ((), ())), preferred_element_type=jnp.float32
    )
    gate_grad = jnp.sum(jax.nn.silu(raised) * backward, axis=1).astype(jnp.bfloat16)
    inner_grad = (backward * silu_slope(raised)).astype(jnp.bfloat16)
    contrib = lax.dot_general(
        inner_grad, up_matrix, (((1,), (1,)), ((), ())), preferred_element_type=jnp.float32
    ).astype(jnp.bfloat16)
    return (contrib, gate_grad)


def exchange(x):
    return lax.all_to_all(x, ("group", "dev"), split_axis=0, concat_axis=0, tiled=True)


def side_block(values, rows):
    n = values.shape[1]
    return jnp.pad(values[:, None, :], ((0, 0), (0, rows - 1), (0, LANES - n)))


def layer(tokens, out_grad, gate_weights, expert_ids, slot_ids, up_weight, down_weight):
    rows_dev = tokens.shape[0]
    features = tokens.shape[1]
    groups = lax.axis_size("group")
    per_group = lax.axis_size("dev")
    experts = groups * per_group
    capacity = 5 * rows_dev * TOPK // (4 * experts)
    slots_all = experts * capacity
    entries = rows_dev * TOPK
    up_matrix = up_weight[0]
    down_matrix = down_weight[0]
    group_of = expert_ids // per_group
    both = 2 * features
    blocks = both // LANES
    part = capacity // CHUNKS
    part_rows = experts * part
    joined = jnp.concatenate(
        [jnp.concatenate([tokens, out_grad], axis=1), jnp.zeros((1, both), jnp.bfloat16)]
    ).reshape(rows_dev + 1, blocks, LANES)
    target = (expert_ids * capacity + slot_ids).reshape(-1)
    slot_table = (
        jnp.full((slots_all,), entries, jnp.int32)
        .at[target]
        .set(jnp.arange(entries, dtype=jnp.int32))
    ).reshape(experts, capacity)
    slot_flat = slot_ids.reshape(-1)
    expert_flat = expert_ids.reshape(-1)
    same_group = group_of == group_of[:, :1]
    selector = jnp.stack([same_group, jnp.logical_not(same_group)], axis=1)
    pick = jnp.where(selector, gate_weights.reshape(rows_dev, 1, TOPK), jnp.bfloat16(0))
    summed = None
    gate_sum = None
    for c in range(CHUNKS):
        table = slot_table[:, c * part:(c + 1) * part]
        sent = joined[table // TOPK].reshape(experts, part * blocks, LANES)
        arrived = exchange(sent)
        data = arrived.reshape(part_rows, both)
        contrib, gate_rows = expert_rows(
            data[:, :features], data[:, features:], up_matrix, down_matrix
        )
        back_blocks = part * features // LANES
        back = jnp.concatenate(
            [
                contrib.reshape(experts, back_blocks, LANES),
                side_block(gate_rows.reshape(experts, part), BACK_ROWS),
            ],
            axis=1,
        )
        returned = exchange(back)
        rows_back = returned[:, :back_blocks, :].reshape(part_rows, features)
        gates_back = returned[:, back_blocks, :part].reshape(part_rows)
        in_chunk = slot_flat // part == c
        spot = jnp.where(in_chunk, expert_flat * part + slot_flat - c * part, -1)
        onehot = (
            spot.reshape(rows_dev, TOPK, 1) == jnp.arange(part_rows, dtype=jnp.int32)
        ).astype(jnp.bfloat16)
        chooser = jnp.einsum(
            "tpk,tkj->tpj", pick, onehot, preferred_element_type=jnp.float32
        ).astype(jnp.bfloat16)
        partial = jnp.einsum("tpj,jd->tpd", chooser, rows_back, preferred_element_type=jnp.float32)
        gate_part = jnp.einsum("tkj,j->tk", onehot, gates_back, preferred_element_type=jnp.float32)
        if c < CHUNKS - 1:
            partial, gate_part = lax.optimization_barrier((partial, gate_part))
        summed = partial if summed is None else summed + partial
        gate_sum = gate_part if gate_sum is None else gate_sum + gate_part
    gate_grad = gate_sum.astype(jnp.bfloat16)
    halves = summed.astype(jnp.bfloat16)
    token_grad = jnp.sum(halves.astype(jnp.float32), axis=1).astype(jnp.bfloat16)
    return (token_grad, gate_grad)


def solution(mesh):
    in_specs = (
        P(("group", "dev"), None),
        P(("group", "dev"), None),
        P(("group", "dev"), None),
        P(("group", "dev"), None),
        P(("group", "dev"), None),
        P(("group", "dev"), None, None),
        P(("group", "dev"), None, None),
    )
    out_specs = (P(("group", "dev"), None), P(("group", "dev"), None))
    return jax.shard_map(layer, mesh=mesh, in_specs=in_specs, out_specs=out_specs, check_vma=False)
```

```python
import jax
import jax.numpy as jnp
from jax import lax
from jax.sharding import PartitionSpec as P

TOPK = 8
LANES = 128


def silu_slope(values):
    sigmoid_up = jax.nn.sigmoid(values)
    return sigmoid_up * (1.0 + values * (1.0 - sigmoid_up))


def expert_rows(token_rows, grad_rows, up_matrix, down_matrix):
    raised = jnp.dot(token_rows, up_matrix, preferred_element_type=jnp.float32)
    backward = lax.dot_general(
        grad_rows, down_matrix, (((1,), (1,)), ((), ())), preferred_element_type=jnp.float32
    )
    gate_grad = jnp.sum(jax.nn.silu(raised) * backward, axis=1).astype(jnp.bfloat16)
    inner_grad = (backward * silu_slope(raised)).astype(jnp.bfloat16)
    contrib = lax.dot_general(
        inner_grad, up_matrix, (((1,), (1,)), ((), ())), preferred_element_type=jnp.float32
    ).astype(jnp.bfloat16)
    return (contrib, gate_grad)


def exchange(x):
    return lax.all_to_all(x, ("group", "dev"), split_axis=0, concat_axis=0, tiled=True)


def side_block(values, rows):
    n = values.shape[1]
    return jnp.pad(values[:, None, :], ((0, 0), (0, rows - 1), (0, LANES - n)))


def layer(tokens, out_grad, gate_weights, expert_ids, slot_ids, up_weight, down_weight):
    rows_dev = tokens.shape[0]
    features = tokens.shape[1]
    groups = lax.axis_size("group")
    per_group = lax.axis_size("dev")
    experts = groups * per_group
    capacity = 5 * rows_dev * TOPK // (4 * experts)
    slots_all = experts * capacity
    entries = rows_dev * TOPK
    up_matrix = up_weight[0]
    down_matrix = down_weight[0]
    group_of = expert_ids // per_group
    both = 2 * features
    blocks = both // LANES
    first = (3 * capacity + 4) // 5
    sizes = (first, capacity - first)
    starts = (0, first)
    joined = jnp.concatenate(
        [jnp.concatenate([tokens, out_grad], axis=1), jnp.zeros((1, both), jnp.bfloat16)]
    ).reshape(rows_dev + 1, blocks, LANES)
    target = (expert_ids * capacity + slot_ids).reshape(-1)
    slot_table = (
        jnp.full((slots_all,), entries, jnp.int32)
        .at[target]
        .set(jnp.arange(entries, dtype=jnp.int32))
    ).reshape(experts, capacity)
    slot_flat = slot_ids.reshape(-1)
    expert_flat = expert_ids.reshape(-1)
    same_group = group_of == group_of[:, :1]
    selector = jnp.stack([same_group, jnp.logical_not(same_group)], axis=1)
    pick = jnp.where(selector, gate_weights.reshape(rows_dev, 1, TOPK), jnp.bfloat16(0))
    summed = None
    gate_sum = None
    for c, (begin, part) in enumerate(zip(starts, sizes)):
        part_rows = experts * part
        table = slot_table[:, begin:begin + part]
        sent = joined[table // TOPK].reshape(experts, part * blocks, LANES)
        arrived = exchange(sent)
        data = arrived.reshape(part_rows, both)
        contrib, gate_rows = expert_rows(
            data[:, :features], data[:, features:], up_matrix, down_matrix
        )
        back_blocks = part * features // LANES
        side_rows = 8 - back_blocks % 8
        back = jnp.concatenate(
            [
                contrib.reshape(experts, back_blocks, LANES),
                side_block(gate_rows.reshape(experts, part), side_rows),
            ],
            axis=1,
        )
        returned = exchange(back)
        rows_back = returned[:, :back_blocks, :].reshape(part_rows, features)
        gates_back = returned[:, back_blocks, :part].reshape(part_rows)
        in_chunk = jnp.logical_and(slot_flat >= begin, slot_flat < begin + part)
        spot = jnp.where(in_chunk, expert_flat * part + slot_flat - begin, -1)
        onehot = (
            spot.reshape(rows_dev, TOPK, 1) == jnp.arange(part_rows, dtype=jnp.int32)
        ).astype(jnp.bfloat16)
        chooser = jnp.einsum(
            "tpk,tkj->tpj", pick, onehot, preferred_element_type=jnp.float32
        ).astype(jnp.bfloat16)
        partial = jnp.einsum("tpj,jd->tpd", chooser, rows_back, preferred_element_type=jnp.float32)
        gate_part = jnp.einsum("tkj,j->tk", onehot, gates_back, preferred_element_type=jnp.float32)
        if c < len(sizes) - 1:
            partial, gate_part = lax.optimization_barrier((partial, gate_part))
        summed = partial if summed is None else summed + partial
        gate_sum = gate_part if gate_sum is None else gate_sum + gate_part
    gate_grad = gate_sum.astype(jnp.bfloat16)
    halves = summed.astype(jnp.bfloat16)
    token_grad = jnp.sum(halves.astype(jnp.float32), axis=1).astype(jnp.bfloat16)
    return (token_grad, gate_grad)


def solution(mesh):
    in_specs = (
        P(("group", "dev"), None),
        P(("group", "dev"), None),
        P(("group", "dev"), None),
        P(("group", "dev"), None),
        P(("group", "dev"), None),
        P(("group", "dev"), None, None),
        P(("group", "dev"), None, None),
    )
    out_specs = (P(("group", "dev"), None), P(("group", "dev"), None))
    return jax.shard_map(layer, mesh=mesh, in_specs=in_specs, out_specs=out_specs, check_vma=False)
```

```python
import jax
import jax.numpy as jnp
from jax import lax
from jax.sharding import PartitionSpec as P

TOPK = 8
LANES = 128
CHUNKS = 2
BACK_ROWS = 4


def silu_slope(values):
    sigmoid_up = jax.nn.sigmoid(values)
    return sigmoid_up * (1.0 + values * (1.0 - sigmoid_up))


def expert_rows(token_rows, grad_rows, up_matrix, down_matrix):
    raised = jnp.dot(token_rows, up_matrix, preferred_element_type=jnp.float32)
    backward = lax.dot_general(
        grad_rows, down_matrix, (((1,), (1,)), ((), ())), preferred_element_type=jnp.float32
    )
    gate_grad = jnp.sum(jax.nn.silu(raised) * backward, axis=1).astype(jnp.bfloat16)
    inner_grad = (backward * silu_slope(raised)).astype(jnp.bfloat16)
    contrib = lax.dot_general(
        inner_grad, up_matrix, (((1,), (1,)), ((), ())), preferred_element_type=jnp.float32
    ).astype(jnp.bfloat16)
    return (contrib, gate_grad)


def exchange(x):
    return lax.all_to_all(x, ("dev", "group"), split_axis=0, concat_axis=0, tiled=True)


def side_block(values, rows):
    n = values.shape[1]
    return jnp.pad(values[:, None, :], ((0, 0), (0, rows - 1), (0, LANES - n)))


def layer(tokens, out_grad, gate_weights, expert_ids, slot_ids, up_weight, down_weight):
    rows_dev = tokens.shape[0]
    features = tokens.shape[1]
    groups = lax.axis_size("group")
    per_group = lax.axis_size("dev")
    experts = groups * per_group
    capacity = 5 * rows_dev * TOPK // (4 * experts)
    slots_all = experts * capacity
    entries = rows_dev * TOPK
    up_matrix = up_weight[0]
    down_matrix = down_weight[0]
    group_of = expert_ids // per_group
    both = 2 * features
    blocks = both // LANES
    part = capacity // CHUNKS
    part_rows = experts * part
    joined = jnp.concatenate(
        [jnp.concatenate([tokens, out_grad], axis=1), jnp.zeros((1, both), jnp.bfloat16)]
    ).reshape(rows_dev + 1, blocks, LANES)
    target = (expert_ids * capacity + slot_ids).reshape(-1)
    slot_table = (
        jnp.full((slots_all,), entries, jnp.int32)
        .at[target]
        .set(jnp.arange(entries, dtype=jnp.int32))
    ).reshape(experts, capacity)
    position = jnp.arange(experts, dtype=jnp.int32)
    slot_table = slot_table[(position % groups) * per_group + position // groups]
    slot_flat = slot_ids.reshape(-1)
    expert_flat = (expert_ids % per_group) * groups + expert_ids // per_group
    expert_flat = expert_flat.reshape(-1)
    same_group = group_of == group_of[:, :1]
    selector = jnp.stack([same_group, jnp.logical_not(same_group)], axis=1)
    pick = jnp.where(selector, gate_weights.reshape(rows_dev, 1, TOPK), jnp.bfloat16(0))
    summed = None
    gate_sum = None
    for c in range(CHUNKS):
        table = slot_table[:, c * part:(c + 1) * part]
        sent = joined[table // TOPK].reshape(experts, part * blocks, LANES)
        arrived = exchange(sent)
        data = arrived.reshape(part_rows, both)
        contrib, gate_rows = expert_rows(
            data[:, :features], data[:, features:], up_matrix, down_matrix
        )
        back_blocks = part * features // LANES
        back = jnp.concatenate(
            [
                contrib.reshape(experts, back_blocks, LANES),
                side_block(gate_rows.reshape(experts, part), BACK_ROWS),
            ],
            axis=1,
        )
        returned = exchange(back)
        rows_back = returned[:, :back_blocks, :].reshape(part_rows, features)
        gates_back = returned[:, back_blocks, :part].reshape(part_rows)
        in_chunk = slot_flat // part == c
        spot = jnp.where(in_chunk, expert_flat * part + slot_flat - c * part, -1)
        onehot = (
            spot.reshape(rows_dev, TOPK, 1) == jnp.arange(part_rows, dtype=jnp.int32)
        ).astype(jnp.bfloat16)
        chooser = jnp.einsum(
            "tpk,tkj->tpj", pick, onehot, preferred_element_type=jnp.float32
        ).astype(jnp.bfloat16)
        partial = jnp.einsum("tpj,jd->tpd", chooser, rows_back, preferred_element_type=jnp.float32)
        gate_part = jnp.einsum("tkj,j->tk", onehot, gates_back, preferred_element_type=jnp.float32)
        if c < CHUNKS - 1:
            partial, gate_part = lax.optimization_barrier((partial, gate_part))
        summed = partial if summed is None else summed + partial
        gate_sum = gate_part if gate_sum is None else gate_sum + gate_part
    gate_grad = gate_sum.astype(jnp.bfloat16)
    halves = summed.astype(jnp.bfloat16)
    token_grad = jnp.sum(halves.astype(jnp.float32), axis=1).astype(jnp.bfloat16)
    return (token_grad, gate_grad)


def solution(mesh):
    in_specs = (
        P(("group", "dev"), None),
        P(("group", "dev"), None),
        P(("group", "dev"), None),
        P(("group", "dev"), None),
        P(("group", "dev"), None),
        P(("group", "dev"), None, None),
        P(("group", "dev"), None, None),
    )
    out_specs = (P(("group", "dev"), None), P(("group", "dev"), None))
    return jax.shard_map(layer, mesh=mesh, in_specs=in_specs, out_specs=out_specs, check_vma=False)
```

```python
import jax
import jax.numpy as jnp
from jax import lax
from jax.sharding import PartitionSpec as P

TOPK = 8
LANES = 128
CHUNKS = 2
BACK_ROWS = 4


def silu_slope(values):
    sigmoid_up = jax.nn.sigmoid(values)
    return sigmoid_up * (1.0 + values * (1.0 - sigmoid_up))


def expert_rows(token_rows, grad_rows, up_matrix, down_matrix):
    raised = jnp.dot(token_rows, up_matrix, preferred_element_type=jnp.float32)
    backward = lax.dot_general(
        grad_rows, down_matrix, (((1,), (1,)), ((), ())), preferred_element_type=jnp.float32
    )
    gate_grad = jnp.sum(jax.nn.silu(raised) * backward, axis=1).astype(jnp.bfloat16)
    inner_grad = (backward * silu_slope(raised)).astype(jnp.bfloat16)
    contrib = lax.dot_general(
        inner_grad, up_matrix, (((1,), (1,)), ((), ())), preferred_element_type=jnp.float32
    ).astype(jnp.bfloat16)
    return (contrib, gate_grad)


def exchange(x):
    return lax.all_to_all(x, ("group", "dev"), split_axis=0, concat_axis=0, tiled=True)


def side_block(values, rows):
    n = values.shape[1]
    return jnp.pad(values[:, None, :], ((0, 0), (0, rows - 1), (0, LANES - n)))


def layer(tokens, out_grad, gate_weights, expert_ids, slot_ids, up_weight, down_weight):
    rows_dev = tokens.shape[0]
    features = tokens.shape[1]
    groups = lax.axis_size("group")
    per_group = lax.axis_size("dev")
    experts = groups * per_group
    capacity = 5 * rows_dev * TOPK // (4 * experts)
    slots_all = experts * capacity
    entries = rows_dev * TOPK
    up_matrix = up_weight[0]
    down_matrix = down_weight[0]
    group_of = expert_ids // per_group
    both = 2 * features
    blocks = both // LANES
    part = capacity // CHUNKS
    part_rows = experts * part
    pair = jnp.concatenate([tokens, out_grad], axis=1).reshape(rows_dev, blocks, LANES)
    target = (expert_ids * capacity + slot_ids).reshape(-1)
    entry = jnp.arange(entries, dtype=jnp.int32)
    slot_table = jnp.min(
        jnp.where(
            target[None, :] == jnp.arange(slots_all, dtype=jnp.int32)[:, None], entry[None, :], entries
        ),
        axis=1,
    ).reshape(experts, capacity)
    slot_flat = slot_ids.reshape(-1)
    expert_flat = expert_ids.reshape(-1)
    same_group = group_of == group_of[:, :1]
    selector = jnp.stack([same_group, jnp.logical_not(same_group)], axis=1)
    pick = jnp.where(selector, gate_weights.reshape(rows_dev, 1, TOPK), jnp.bfloat16(0))
    summed = None
    gate_sum = None
    for c in range(CHUNKS):
        table = slot_table[:, c * part:(c + 1) * part]
        anchor = table // TOPK
        rows = pair[jnp.minimum(anchor, rows_dev - 1)]
        sent = jnp.where((anchor < rows_dev)[:, :, None, None], rows.reshape(experts, part, blocks, LANES), 0)
        sent = sent.astype(jnp.bfloat16).reshape(experts, part * blocks, LANES)
        arrived = exchange(sent)
        data = arrived.reshape(part_rows, both)
        contrib, gate_rows = expert_rows(
            data[:, :features], data[:, features:], up_matrix, down_matrix
        )
        back_blocks = part * features // LANES
        back = jnp.concatenate(
            [
                contrib.reshape(experts, back_blocks, LANES),
                side_block(gate_rows.reshape(experts, part), BACK_ROWS),
            ],
            axis=1,
        )
        returned = exchange(back)
        rows_back = returned[:, :back_blocks, :].reshape(part_rows, features)
        gates_back = returned[:, back_blocks, :part].reshape(part_rows)
        in_chunk = slot_flat // part == c
        spot = jnp.where(in_chunk, expert_flat * part + slot_flat - c * part, -1)
        onehot = (
            spot.reshape(rows_dev, TOPK, 1) == jnp.arange(part_rows, dtype=jnp.int32)
        ).astype(jnp.bfloat16)
        chooser = jnp.einsum(
            "tpk,tkj->tpj", pick, onehot, preferred_element_type=jnp.float32
        ).astype(jnp.bfloat16)
        partial = jnp.einsum("tpj,jd->tpd", chooser, rows_back, preferred_element_type=jnp.float32)
        gate_part = jnp.einsum("tkj,j->tk", onehot, gates_back, preferred_element_type=jnp.float32)
        if c < CHUNKS - 1:
            partial, gate_part = lax.optimization_barrier((partial, gate_part))
        summed = partial if summed is None else summed + partial
        gate_sum = gate_part if gate_sum is None else gate_sum + gate_part
    gate_grad = gate_sum.astype(jnp.bfloat16)
    halves = summed.astype(jnp.bfloat16)
    token_grad = jnp.sum(halves.astype(jnp.float32), axis=1).astype(jnp.bfloat16)
    return (token_grad, gate_grad)


def solution(mesh):
    in_specs = (
        P(("group", "dev"), None),
        P(("group", "dev"), None),
        P(("group", "dev"), None),
        P(("group", "dev"), None),
        P(("group", "dev"), None),
        P(("group", "dev"), None, None),
        P(("group", "dev"), None, None),
    )
    out_specs = (P(("group", "dev"), None), P(("group", "dev"), None))
    return jax.shard_map(layer, mesh=mesh, in_specs=in_specs, out_specs=out_specs, check_vma=False)
```

```python
import jax
import jax.numpy as jnp
from jax import lax
from jax.sharding import PartitionSpec as P

TOPK = 8
LANES = 128
CHUNKS = 2
BACK_ROWS = 4


def silu_slope(values):
    sigmoid_up = jax.nn.sigmoid(values)
    return sigmoid_up * (1.0 + values * (1.0 - sigmoid_up))


def expert_rows(token_rows, grad_rows, up_matrix, down_matrix):
    raised = jnp.dot(token_rows, up_matrix, preferred_element_type=jnp.float32)
    backward = lax.dot_general(
        grad_rows, down_matrix, (((1,), (1,)), ((), ())), preferred_element_type=jnp.float32
    )
    gate_grad = jnp.sum(jax.nn.silu(raised) * backward, axis=1).astype(jnp.bfloat16)
    inner_grad = (backward * silu_slope(raised)).astype(jnp.bfloat16)
    contrib = lax.dot_general(
        inner_grad, up_matrix, (((1,), (1,)), ((), ())), preferred_element_type=jnp.float32
    ).astype(jnp.bfloat16)
    return (contrib, gate_grad)


def exchange(x):
    return lax.all_to_all(x, ("group", "dev"), split_axis=0, concat_axis=0, tiled=True)


def side_block(values, rows):
    n = values.shape[1]
    return jnp.pad(values[:, None, :], ((0, 0), (0, rows - 1), (0, LANES - n)))


def layer(tokens, out_grad, gate_weights, expert_ids, slot_ids, up_weight, down_weight):
    rows_dev = tokens.shape[0]
    features = tokens.shape[1]
    groups = lax.axis_size("group")
    per_group = lax.axis_size("dev")
    experts = groups * per_group
    capacity = 5 * rows_dev * TOPK // (4 * experts)
    slots_all = experts * capacity
    entries = rows_dev * TOPK
    up_matrix = up_weight[0]
    down_matrix = down_weight[0]
    group_of = expert_ids // per_group
    both = 2 * features
    blocks = both // LANES
    part = capacity // CHUNKS
    part_rows = experts * part
    joined = jnp.concatenate(
        [jnp.concatenate([tokens, out_grad], axis=1), jnp.zeros((1, both), jnp.bfloat16)]
    ).reshape(rows_dev + 1, blocks, LANES)
    target = (expert_ids * capacity + slot_ids).reshape(-1)
    entry = jnp.arange(entries, dtype=jnp.int32)
    slot_table = jnp.min(
        jnp.where(
            target[None, :] == jnp.arange(slots_all, dtype=jnp.int32)[:, None], entry[None, :], entries
        ),
        axis=1,
    ).reshape(experts, capacity)
    slot_flat = slot_ids.reshape(-1)
    expert_flat = expert_ids.reshape(-1)
    same_group = group_of == group_of[:, :1]
    selector = jnp.stack([same_group, jnp.logical_not(same_group)], axis=1)
    pick = jnp.where(selector, gate_weights.reshape(rows_dev, 1, TOPK), jnp.bfloat16(0))
    summed = None
    gate_sum = None
    for c in range(CHUNKS):
        table = slot_table[:, c * part:(c + 1) * part]
        sent = joined[table // TOPK].reshape(experts, part * blocks, LANES)
        arrived = exchange(sent)
        data = arrived.reshape(part_rows, both)
        contrib, gate_rows = expert_rows(
            data[:, :features], data[:, features:], up_matrix, down_matrix
        )
        back_blocks = part * features // LANES
        back = jnp.concatenate(
            [
                contrib.reshape(experts, back_blocks, LANES),
                side_block(gate_rows.reshape(experts, part), BACK_ROWS),
            ],
            axis=1,
        )
        returned = exchange(back)
        in_chunk = slot_flat // part == c
        spot = jnp.where(in_chunk, expert_flat * part + slot_flat - c * part, -1)
        onehot = (
            spot.reshape(rows_dev, TOPK, 1) == jnp.arange(part_rows, dtype=jnp.int32)
        ).astype(jnp.bfloat16)
        chooser = jnp.einsum(
            "tpk,tkj->tpj", pick, onehot, preferred_element_type=jnp.float32
        ).astype(jnp.bfloat16)
        onehot, chooser = lax.optimization_barrier((onehot, chooser))
        rows_back = returned[:, :back_blocks, :].reshape(part_rows, features)
        gates_back = returned[:, back_blocks, :part].reshape(part_rows)
        partial = jnp.einsum("tpj,jd->tpd", chooser, rows_back, preferred_element_type=jnp.float32)
        gate_part = jnp.einsum("tkj,j->tk", onehot, gates_back, preferred_element_type=jnp.float32)
        if c < CHUNKS - 1:
            partial, gate_part = lax.optimization_barrier((partial, gate_part))
        summed = partial if summed is None else summed + partial
        gate_sum = gate_part if gate_sum is None else gate_sum + gate_part
    gate_grad = gate_sum.astype(jnp.bfloat16)
    halves = summed.astype(jnp.bfloat16)
    token_grad = jnp.sum(halves.astype(jnp.float32), axis=1).astype(jnp.bfloat16)
    return (token_grad, gate_grad)


def solution(mesh):
    in_specs = (
        P(("group", "dev"), None),
        P(("group", "dev"), None),
        P(("group", "dev"), None),
        P(("group", "dev"), None),
        P(("group", "dev"), None),
        P(("group", "dev"), None, None),
        P(("group", "dev"), None, None),
    )
    out_specs = (P(("group", "dev"), None), P(("group", "dev"), None))
    return jax.shard_map(layer, mesh=mesh, in_specs=in_specs, out_specs=out_specs, check_vma=False)
```

```python
import jax
import jax.numpy as jnp
from jax import lax
from jax.sharding import PartitionSpec as P

TOPK = 8
LANES = 128
CHUNKS = 2
BACK_ROWS = 4


def silu_slope(values):
    sigmoid_up = jax.nn.sigmoid(values)
    return sigmoid_up * (1.0 + values * (1.0 - sigmoid_up))


def expert_rows(token_rows, grad_rows, up_matrix, down_matrix):
    raised = jnp.dot(token_rows, up_matrix, preferred_element_type=jnp.float32)
    backward = lax.dot_general(
        grad_rows, down_matrix, (((1,), (1,)), ((), ())), preferred_element_type=jnp.float32
    )
    gate_grad = jnp.sum(jax.nn.silu(raised) * backward, axis=1).astype(jnp.bfloat16)
    inner_grad = (backward * silu_slope(raised)).astype(jnp.bfloat16)
    contrib = lax.dot_general(
        inner_grad, up_matrix, (((1,), (1,)), ((), ())), preferred_element_type=jnp.float32
    ).astype(jnp.bfloat16)
    return (contrib, gate_grad)


def exchange(x):
    return lax.all_to_all(x, ("group", "dev"), split_axis=0, concat_axis=0, tiled=True)


def side_block(values, rows):
    n = values.shape[1]
    return jnp.pad(values[:, None, :], ((0, 0), (0, rows - 1), (0, LANES - n)))


def layer(tokens, out_grad, gate_weights, expert_ids, slot_ids, up_weight, down_weight):
    rows_dev = tokens.shape[0]
    features = tokens.shape[1]
    groups = lax.axis_size("group")
    per_group = lax.axis_size("dev")
    experts = groups * per_group
    capacity = 5 * rows_dev * TOPK // (4 * experts)
    slots_all = experts * capacity
    entries = rows_dev * TOPK
    up_matrix = up_weight[0]
    down_matrix = down_weight[0]
    group_of = expert_ids // per_group
    both = 2 * features
    blocks = both // LANES
    part = capacity // CHUNKS
    part_rows = experts * part
    joined = jnp.concatenate(
        [jnp.concatenate([tokens, out_grad], axis=1), jnp.zeros((1, both), jnp.bfloat16)]
    ).reshape(rows_dev + 1, blocks, LANES)
    target = (expert_ids * capacity + slot_ids).reshape(-1)
    entry = jnp.arange(entries, dtype=jnp.int32)
    slot_table = jnp.min(
        jnp.where(
            target[None, :] == jnp.arange(slots_all, dtype=jnp.int32)[:, None], entry[None, :], entries
        ),
        axis=1,
    ).reshape(experts, capacity)
    slot_flat = slot_ids.reshape(-1)
    expert_flat = expert_ids.reshape(-1)
    same_group = group_of == group_of[:, :1]
    selector = jnp.stack([same_group, jnp.logical_not(same_group)], axis=1)
    pick = jnp.where(selector, gate_weights.reshape(rows_dev, 1, TOPK), jnp.bfloat16(0))
    summed = None
    gate_sum = None
    for c in range(CHUNKS):
        table = slot_table[:, c * part:(c + 1) * part]
        sent = joined[table // TOPK].reshape(experts, part * blocks, LANES)
        arrived = exchange(sent)
        data = arrived.reshape(part_rows, both)
        contrib, gate_rows = expert_rows(
            data[:, :features], data[:, features:], up_matrix, down_matrix
        )
        back_blocks = part * features // LANES
        back = jnp.concatenate(
            [
                contrib.reshape(experts, back_blocks, LANES),
                side_block(gate_rows.reshape(experts, part), BACK_ROWS),
            ],
            axis=1,
        )
        returned = exchange(back)
        rows_back = returned[:, :back_blocks, :].reshape(part_rows, features)
        gate_block = returned[:, back_blocks, :]
        in_chunk = slot_flat // part == c
        spot = jnp.where(in_chunk, expert_flat * part + slot_flat - c * part, -1)
        onehot = (
            spot.reshape(rows_dev, TOPK, 1) == jnp.arange(part_rows, dtype=jnp.int32)
        ).astype(jnp.bfloat16)
        chooser = jnp.einsum(
            "tpk,tkj->tpj", pick, onehot, preferred_element_type=jnp.float32
        ).astype(jnp.bfloat16)
        partial = jnp.einsum("tpj,jd->tpd", chooser, rows_back, preferred_element_type=jnp.float32)
        expert_hot = jnp.logical_and(
            expert_flat[:, None] == jnp.arange(experts, dtype=jnp.int32), in_chunk[:, None]
        ).astype(jnp.bfloat16)
        gate_rows_of = jnp.dot(expert_hot, gate_block, preferred_element_type=jnp.float32)
        lane = (slot_flat - c * part)[:, None] == jnp.arange(LANES, dtype=jnp.int32)
        gate_part = jnp.sum(jnp.where(lane, gate_rows_of, 0.0), axis=1).reshape(rows_dev, TOPK)
        if c < CHUNKS - 1:
            partial, gate_part = lax.optimization_barrier((partial, gate_part))
        summed = partial if summed is None else summed + partial
        gate_sum = gate_part if gate_sum is None else gate_sum + gate_part
    gate_grad = gate_sum.astype(jnp.bfloat16)
    halves = summed.astype(jnp.bfloat16)
    token_grad = jnp.sum(halves.astype(jnp.float32), axis=1).astype(jnp.bfloat16)
    return (token_grad, gate_grad)


def solution(mesh):
    in_specs = (
        P(("group", "dev"), None),
        P(("group", "dev"), None),
        P(("group", "dev"), None),
        P(("group", "dev"), None),
        P(("group", "dev"), None),
        P(("group", "dev"), None, None),
        P(("group", "dev"), None, None),
    )
    out_specs = (P(("group", "dev"), None), P(("group", "dev"), None))
    return jax.shard_map(layer, mesh=mesh, in_specs=in_specs, out_specs=out_specs, check_vma=False)
```
